256 devices in a mesh: tm: 64 (over x, z_lo, y), feed: 4 (over z_hi, core).
Axes of the slice: x: 4, y: 4, z: 8 (z_hi: 2, z_lo: 4; z = z_hi * 4 + z_lo), core: 2. Of those that a mesh axis runs over, the one named last changes fastest.
Arguments:
- voltages: bfloat16 [1024, 131072], P('feed', 'tm'), may hold values from -6 to 6
- coefficients: float32 [16, 2048], replicated, may hold values from -1.5 to 1.5
- beam_weights: bfloat16 [1024, 1024, 2, 512], P('tm', 'feed'), may hold values from -0.1875 to 0.1875
Outputs:
- beam_power: float32 [8, 1024, 512], P(None, 'tm', 'feed')
The draws below stay inside these ranges and needn't reach their ends.
All inputs are finite; a program needn't handle non-finite values.
Results may differ from the reference program's by a relative error of at most 0.0025.
Values may be sent and summed in bfloat16 or wider, within the bound.
No kernel may reach another device: no remote copies, remote signals or barrier semaphores. Data moves between devices by JAX's collectives and lax.ppermute only.
A program may use at most 128 MiB of HBM per device.

```python
import math
import jax
import jax.numpy as jnp
from jax import lax

FEEDS = 1024
CH = 1024
BEAMS = 512
TAPS = 16
INTEG = 8
FRAME = 2048
FRAMES = 64
N_TM = 64
N_FEED = 4


def with_spikes(drawn, own_key, source, target, blocks, factor):
    def block_of(position):
        return (jnp.arange(drawn.shape[position]) // (drawn.shape[position] // blocks)).reshape((-1,) + (1,) * (drawn.ndim - 1 - position))

    one_side = jax.random.permutation(own_key, blocks)[block_of(target)]
    far = (block_of(target) + blocks // 2) % blocks
    return jnp.where((block_of(source) == one_side) | (block_of(source) == far), factor * drawn, drawn)


def steps_of(own_key, shape, cuts, least, high):
    factor_of = 1.0
    for position, shards_of in cuts:
        draws = jax.random.uniform(jax.random.fold_in(jax.random.fold_in(own_key, 6), position), (shards_of,), jnp.float32, least / len(cuts), high / len(cuts))
        factor_of = factor_of * jnp.repeat(jnp.exp(draws), shape[position] // shards_of).reshape((-1,) + (1,) * (len(shape) - 1 - position))
    return factor_of


def noise(rng, dims, width, limit, pieces=(), kind=jnp.bfloat16):
    loudness = steps_of(rng, dims, pieces, -0.22, 0.18) if pieces else 1.0
    drawn = jax.random.normal(rng, dims, jnp.float32) * width * loudness
    return jnp.minimum(jnp.maximum(drawn, -limit), limit).astype(kind)


def noise_with(rng, shape, width, bound, split, heavy, kind=jnp.bfloat16):
    drawn = width * jax.random.normal(rng, shape, jnp.float32)
    if split:
        drawn = drawn * steps_of(rng, shape, split, -0.22, 0.18)
    return jnp.clip(with_spikes(drawn, jax.random.fold_in(rng, 3), *heavy), -bound, bound).astype(kind)


def setup_inputs(seed: int = 0) -> dict:
    splits = jax.random.split(jax.random.key(seed), 4)
    return {
        "voltages": noise(splits[0], (FEEDS, FRAMES * FRAME), 1.0, 6.0, ((0, 4), (1, 64))),
        "coefficients": noise(splits[1], (TAPS, FRAME), 0.25, 1.5, (), jnp.float32),
        "beam_weights": noise_with(splits[2], (CH, FEEDS, 2, BEAMS), (2 * FEEDS) ** -0.5, 0.1875, ((0, 64), (1, 4)), (1, 3, 4, 2.0)),
    }


def dft_table(frame_len):
    channels = frame_len // 2
    sample = lax.broadcasted_iota(jnp.int32, (frame_len, channels), 0)
    channel = lax.broadcasted_iota(jnp.int32, (frame_len, channels), 1)
    angles = 2.0 * math.pi / frame_len * (sample * channel % frame_len).astype(jnp.float32)
    norming = 1.0 / math.sqrt(frame_len)
    stacked = jnp.stack([jnp.cos(angles) * norming, -jnp.sin(angles) * norming], axis=2)
    return stacked.reshape(frame_len, 2 * channels).astype(jnp.bfloat16)

def polyphase(extended, coefficients, frames):
    tap_count = coefficients.shape[0]
    running = jnp.zeros((extended.shape[0], frames, extended.shape[2]), jnp.float32)
    for tap_index in range(tap_count):
        running = running + coefficients[tap_index][None, None, :] * extended[:, tap_index:tap_index + frames, :].astype(jnp.float32)
    return running.astype(jnp.bfloat16)

def combine_weights(real_w, imag_w):
    first = jnp.stack([real_w, imag_w], axis=2)
    second = jnp.stack([-imag_w, real_w], axis=2)
    return jnp.stack([first, second], axis=2)

def reference(voltages, coefficients, beam_weights):
    tap_count, frame_len = coefficients.shape
    transform = dft_table(frame_len)
    feed_slab = FEEDS // N_FEED
    grouped = voltages.reshape(N_FEED, feed_slab, FRAMES, frame_len)

    def channelize(feed_block):
        padded = jnp.concatenate([feed_block, jnp.zeros((feed_slab, tap_count - 1, frame_len), jnp.bfloat16)], axis=1)
        filtered = polyphase(padded, coefficients, FRAMES)
        flat = filtered.reshape(feed_slab * FRAMES, frame_len)
        result = jnp.dot(flat, transform, preferred_element_type=jnp.float32).astype(jnp.bfloat16)
        return result.reshape(feed_slab, FRAMES, 2 * CH)
    spectra = lax.map(channelize, grouped).reshape(FEEDS, FRAMES, 2 * CH)
    per_group = CH // N_TM
    arranged = jnp.transpose(spectra.reshape(FEEDS, FRAMES, N_TM, per_group, 2), (2, 1, 3, 4, 0))
    weights_grouped = beam_weights.reshape(N_TM, per_group, FEEDS, 2, BEAMS)

    def form(pair):
        spectrum_block, weight_block = pair
        combined = combine_weights(weight_block[:, :, 0], weight_block[:, :, 1])
        beams = jnp.einsum('tcrf,cfrsb->bsct', spectrum_block.astype(jnp.float32), combined.astype(jnp.float32))
        energy = lax.optimization_barrier(jnp.sum(beams * beams, axis=1))
        binned = lax.optimization_barrier(jnp.mean(energy.reshape(BEAMS, per_group, FRAMES // INTEG, INTEG), axis=3))
        return jnp.transpose(binned, (2, 1, 0))
    powers = lax.map(form, (arranged, weights_grouped))
    return jnp.transpose(powers, (1, 0, 2, 3)).reshape(FRAMES // INTEG, CH, BEAMS)
```

```python
import math

import jax
import jax.numpy as jnp
from jax import lax
from jax.sharding import PartitionSpec as P

INTEG = 8


def dft_table(frame_len):
    channels = frame_len // 2
    sample = lax.broadcasted_iota(jnp.int32, (frame_len, channels), 0)
    channel = lax.broadcasted_iota(jnp.int32, (frame_len, channels), 1)
    angles = 2.0 * math.pi / frame_len * (sample * channel % frame_len).astype(jnp.float32)
    norming = 1.0 / math.sqrt(frame_len)
    stacked = jnp.stack([jnp.cos(angles) * norming, -jnp.sin(angles) * norming], axis=2)
    return stacked.reshape(frame_len, 2 * channels).astype(jnp.bfloat16)


def polyphase(extended, coefficients, frames):
    tap_count = coefficients.shape[0]
    running = jnp.zeros((extended.shape[0], frames, extended.shape[2]), jnp.float32)
    for tap_index in range(tap_count):
        running = running + coefficients[tap_index][None, None, :] * extended[
            :, tap_index : tap_index + frames, :
        ].astype(jnp.float32)
    return running.astype(jnp.bfloat16)


def local(voltages, coefficients, beam_weights):
    n_tm = lax.axis_size("tm")
    feeds_here, samples = voltages.shape
    tap_count, frame_len = coefficients.shape
    frames_here = samples // frame_len
    total_frames = n_tm * frames_here
    per_dev = feeds_here // n_tm

    blocks = voltages.reshape(n_tm, per_dev, samples)
    blocks = lax.all_to_all(blocks, "tm", 0, 0, tiled=True)
    frames = blocks.reshape(n_tm, per_dev, frames_here, frame_len)
    frames = jnp.transpose(frames, (1, 0, 2, 3)).reshape(per_dev, total_frames, frame_len)
    padding = jnp.zeros((per_dev, tap_count - 1, frame_len), frames.dtype)
    extended = jnp.concatenate([frames, padding], axis=1)
    filtered = polyphase(extended, coefficients, total_frames)

    transform = dft_table(frame_len)
    spectra = jnp.dot(
        filtered.reshape(per_dev * total_frames, frame_len),
        transform,
        preferred_element_type=jnp.float32,
    ).astype(jnp.bfloat16)
    cols = transform.shape[1]
    group_cols = cols // n_tm
    spectra = spectra.reshape(per_dev, total_frames, n_tm, group_cols)
    spectra = jnp.transpose(spectra, (2, 0, 1, 3))
    turned = lax.all_to_all(spectra, "tm", 0, 0, tiled=True)
    per_group = group_cols // 2
    turned = turned.reshape(feeds_here, total_frames, per_group, 2)
    real_part = turned[..., 0]
    imag_part = turned[..., 1]
    for_real = jnp.stack([real_part, -imag_part], axis=3)
    for_imag = jnp.stack([imag_part, real_part], axis=3)
    paired = jnp.stack([for_real, for_imag], axis=0)
    paired = jnp.transpose(paired, (3, 0, 2, 1, 4)).reshape(
        per_group, 2 * total_frames, feeds_here * 2
    )
    weights = beam_weights.reshape(per_group, feeds_here * 2, beam_weights.shape[3])
    beams = jnp.einsum("cmk,ckb->bcm", paired, weights, preferred_element_type=jnp.float32)
    beams = lax.psum_scatter(beams, "feed", scatter_dimension=0, tiled=True)
    beams = beams.reshape(beams.shape[0], per_group, 2, total_frames)
    energy = jnp.sum(beams * beams, axis=2)
    binned = jnp.mean(
        energy.reshape(energy.shape[0], per_group, total_frames // INTEG, INTEG), axis=3
    )
    return jnp.transpose(binned, (2, 1, 0))


def solution(mesh):
    placed = (P("feed", "tm"), P(), P("tm", "feed", None, None))
    return jax.shard_map(
        local, mesh=mesh, in_specs=placed, out_specs=P(None, "tm", "feed"), check_vma=False
    )
```

```python
import math

import jax
import jax.numpy as jnp
from jax import lax
from jax.sharding import PartitionSpec as P

INTEG = 8


def dft_rows(frame_len, n_groups):
    channels = frame_len // 2
    inner = 64
    outer = frame_len // inner
    cols = 2 * channels
    col = lax.broadcasted_iota(jnp.int32, (cols, 1), 0)
    per_group = channels // n_groups
    group = col // (2 * per_group)
    channel = group * per_group + (col % (2 * per_group)) // 2
    part = col % 2
    step = 2.0 * math.pi / frame_len
    high = lax.broadcasted_iota(jnp.int32, (1, outer), 1)
    low = lax.broadcasted_iota(jnp.int32, (1, inner), 1)
    high_angle = step * ((inner * high * channel) % frame_len).astype(jnp.float32)
    low_angle = step * ((low * channel) % frame_len).astype(jnp.float32)
    cos_high = jnp.cos(high_angle)
    sin_high = jnp.sin(high_angle)
    first = jnp.where(part == 0, cos_high, -sin_high)
    second = jnp.where(part == 0, sin_high, cos_high)
    cos_low = jnp.cos(low_angle)
    sin_low = jnp.sin(low_angle)
    norming = 1.0 / math.sqrt(frame_len)
    table = (
        first[:, :, None] * cos_low[:, None, :] - second[:, :, None] * sin_low[:, None, :]
    ) * norming
    return table.reshape(cols, frame_len).astype(jnp.bfloat16)


def polyphase(extended, coefficients, frames):
    tap_count = coefficients.shape[0]
    running = jnp.zeros((extended.shape[0], frames, extended.shape[2]), jnp.float32)
    for tap_index in range(tap_count):
        running = running + coefficients[tap_index][None, None, :] * extended[
            :, tap_index : tap_index + frames, :
        ].astype(jnp.float32)
    return running.astype(jnp.bfloat16)


def halve(value, axis, flip):
    count = lax.axis_size(axis)
    own = lax.axis_index(axis) // flip % 2
    pairs = [(i, i ^ flip) for i in range(count)]
    above = count // (2 * flip)
    lead = value.shape[0]
    split = value.reshape(above, 2, lead // (2 * above), *value.shape[1:])
    kept = lax.dynamic_index_in_dim(split, own, 1, keepdims=False)
    sent = lax.dynamic_index_in_dim(split, 1 - own, 1, keepdims=False)
    summed = kept + lax.ppermute(sent, axis, pairs)
    return summed.reshape(lead // 2, *value.shape[1:])


def local(voltages, coefficients, beam_weights):
    n_tm = lax.axis_size("tm")
    n_feed = lax.axis_size("feed")
    feeds_here, samples = voltages.shape
    tap_count, frame_len = coefficients.shape
    frames_here = samples // frame_len
    total_frames = n_tm * frames_here
    per_dev = feeds_here // n_tm

    blocks = voltages.reshape(n_tm, per_dev, samples)
    blocks = lax.all_to_all(blocks, "tm", 0, 0, tiled=True)
    frames = blocks.reshape(n_tm, per_dev, frames_here, frame_len)
    frames = jnp.transpose(frames, (1, 0, 2, 3)).reshape(per_dev, total_frames, frame_len)
    padding = jnp.zeros((per_dev, tap_count - 1, frame_len), frames.dtype)
    extended = jnp.concatenate([frames, padding], axis=1)
    filtered = polyphase(extended, coefficients, total_frames)

    table = dft_rows(frame_len, n_tm)
    spectra = jnp.einsum(
        "jk,mk->jm",
        table,
        filtered.reshape(per_dev * total_frames, frame_len),
        preferred_element_type=jnp.float32,
    ).astype(jnp.bfloat16)
    cols = table.shape[0]
    group_cols = cols // n_tm
    per_group = group_cols // 2
    spectra = spectra.reshape(n_tm, group_cols, per_dev * total_frames)
    turned = lax.all_to_all(spectra, "tm", 0, 0, tiled=True)
    turned = turned.reshape(n_tm, per_group, 2, per_dev, total_frames)
    turned = jnp.transpose(turned, (1, 0, 3, 2, 4)).reshape(per_group, feeds_here, 2, total_frames)
    real_part = turned[:, :, 0]
    imag_part = turned[:, :, 1]
    for_real = jnp.stack([real_part, -imag_part], axis=2)
    for_imag = jnp.stack([imag_part, real_part], axis=2)
    paired = jnp.concatenate([for_real, for_imag], axis=3).reshape(
        per_group, feeds_here * 2, 2 * total_frames
    )
    weights = beam_weights.reshape(per_group, feeds_here * 2, beam_weights.shape[3])
    beams = jnp.einsum("ckb,ckn->bcn", weights, paired, preferred_element_type=jnp.float32)
    flip = 1
    while flip < n_feed:
        beams = halve(beams, "feed", flip)
        flip *= 2
    beams = beams.reshape(beams.shape[0], per_group, 2, total_frames)
    energy = jnp.sum(beams * beams, axis=2)
    binned = jnp.mean(
        energy.reshape(energy.shape[0], per_group, total_frames // INTEG, INTEG), axis=3
    )
    return jnp.transpose(binned, (2, 1, 0))


def solution(mesh):
    placed = (P("feed", "tm"), P(), P("tm", "feed", None, None))
    return jax.shard_map(
        local, mesh=mesh, in_specs=placed, out_specs=P(None, "tm", "feed"), check_vma=False
    )
```

```python
import math

import jax
import jax.numpy as jnp
from jax import lax
from jax.sharding import PartitionSpec as P

INTEG = 8


def dft_rows(frame_len, n_groups, n_halves):
    channels = frame_len // 2
    inner = 64
    outer = frame_len // inner
    cols = 2 * channels
    col = lax.broadcasted_iota(jnp.int32, (cols, 1), 0)
    per_group = channels // n_groups
    per_half = per_group // n_halves
    half = col // (2 * channels // n_halves)
    group = col % (2 * channels // n_halves) // (2 * per_half)
    channel = group * per_group + half * per_half + (col % (2 * per_half)) // 2
    part = col % 2
    step = 2.0 * math.pi / frame_len
    high = lax.broadcasted_iota(jnp.int32, (1, outer), 1)
    low = lax.broadcasted_iota(jnp.int32, (1, inner), 1)
    high_angle = step * ((inner * high * channel) % frame_len).astype(jnp.float32)
    low_angle = step * ((low * channel) % frame_len).astype(jnp.float32)
    cos_high = jnp.cos(high_angle)
    sin_high = jnp.sin(high_angle)
    first = jnp.where(part == 0, cos_high, -sin_high)
    second = jnp.where(part == 0, sin_high, cos_high)
    cos_low = jnp.cos(low_angle)
    sin_low = jnp.sin(low_angle)
    norming = 1.0 / math.sqrt(frame_len)
    table = (
        first[:, :, None] * cos_low[:, None, :] - second[:, :, None] * sin_low[:, None, :]
    ) * norming
    return table.reshape(cols, frame_len).astype(jnp.bfloat16)


def polyphase(extended, coefficients, frames):
    tap_count = coefficients.shape[0]
    running = jnp.zeros((extended.shape[0], frames, extended.shape[2]), jnp.float32)
    for tap_index in range(tap_count):
        running = running + coefficients[tap_index][None, None, :] * extended[
            :, tap_index : tap_index + frames, :
        ].astype(jnp.float32)
    return running.astype(jnp.bfloat16)


def exchange(blocks, axis, flip):
    count = lax.axis_size(axis)
    bit = lax.axis_index(axis) // flip % 2
    from_low = [(i, i ^ flip) for i in range(count) if i // flip % 2 == 0]
    from_high = [(i, i ^ flip) for i in range(count) if i // flip % 2 == 1]
    to_high = lax.ppermute(blocks[1], axis, from_low)
    to_low = lax.ppermute(blocks[0], axis, from_high)
    return jnp.where(bit == 0, blocks[0], blocks[1]) + to_high + to_low


def local(voltages, coefficients, beam_weights):
    n_tm = lax.axis_size("tm")
    n_feed = lax.axis_size("feed")
    feeds_here, samples = voltages.shape
    tap_count, frame_len = coefficients.shape
    frames_here = samples // frame_len
    total_frames = n_tm * frames_here
    per_dev = feeds_here // n_tm

    blocks = voltages.reshape(n_tm, per_dev, samples)
    blocks = lax.all_to_all(blocks, "tm", 0, 0, tiled=True)
    frames = blocks.reshape(n_tm, per_dev, frames_here, frame_len)
    frames = jnp.transpose(frames, (1, 0, 2, 3)).reshape(per_dev, total_frames, frame_len)
    padding = jnp.zeros((per_dev, tap_count - 1, frame_len), frames.dtype)
    extended = jnp.concatenate([frames, padding], axis=1)
    filtered = polyphase(extended, coefficients, total_frames)

    n_halves = 2
    table = dft_rows(frame_len, n_tm, n_halves)
    cols = table.shape[0]
    group_cols = cols // n_tm // n_halves
    per_half = group_cols // 2
    samples_flat = filtered.reshape(per_dev * total_frames, frame_len)
    beam_count = beam_weights.shape[3]
    per_out = beam_count // n_feed
    binned_parts = []
    for half in range(n_halves):
        rows = table[half * (cols // n_halves) : (half + 1) * (cols // n_halves)]
        spectra = jnp.einsum(
            "jk,mk->jm", rows, samples_flat, preferred_element_type=jnp.float32
        ).astype(jnp.bfloat16)
        spectra = spectra.reshape(n_tm, group_cols, per_dev * total_frames)
        turned = lax.all_to_all(spectra, "tm", 0, 0, tiled=True)
        turned = turned.reshape(n_tm, per_half, 2, per_dev, total_frames)
        turned = jnp.transpose(turned, (1, 0, 3, 2, 4)).reshape(
            per_half, feeds_here, 2, total_frames
        )
        real_part = turned[:, :, 0]
        imag_part = turned[:, :, 1]
        for_real = jnp.stack([real_part, -imag_part], axis=2)
        for_imag = jnp.stack([imag_part, real_part], axis=2)
        paired = jnp.concatenate([for_real, for_imag], axis=3).reshape(
            per_half, feeds_here * 2, 2 * total_frames
        )
        weights = beam_weights[half * per_half : (half + 1) * per_half].reshape(
            per_half, feeds_here * 2, n_feed, per_out
        )
        beams = jnp.einsum("ckjb,ckn->jcbn", weights, paired, preferred_element_type=jnp.float32)
        flip = 1
        while flip < n_feed:
            split = beams.reshape(-1, 2, *beams.shape[1:])
            beams = exchange((split[:, 0], split[:, 1]), "feed", flip).reshape(
                -1, *beams.shape[1:]
            )
            flip *= 2
        summed = beams[0].reshape(per_half, per_out, 2, total_frames)
        energy = jnp.sum(summed * summed, axis=2)
        binned_parts.append(
            jnp.mean(energy.reshape(per_half, per_out, total_frames // INTEG, INTEG), axis=3)
        )
    binned = jnp.concatenate(binned_parts, axis=0)
    return jnp.transpose(binned, (2, 0, 1))


def solution(mesh):
    placed = (P("feed", "tm"), P(), P("tm", "feed", None, None))
    return jax.shard_map(
        local, mesh=mesh, in_specs=placed, out_specs=P(None, "tm", "feed"), check_vma=False
    )
```

```python
import math

import jax
import jax.numpy as jnp
from jax import lax
from jax.sharding import PartitionSpec as P

INTEG = 8


def dft_rows(frame_len, n_groups):
    channels = frame_len // 2
    inner = 64
    outer = frame_len // inner
    cols = 2 * channels
    col = lax.broadcasted_iota(jnp.int32, (cols, 1), 0)
    per_group = channels // n_groups
    group = col // (2 * per_group)
    channel = group * per_group + (col % (2 * per_group)) // 2
    part = col % 2
    step = 2.0 * math.pi / frame_len
    high = lax.broadcasted_iota(jnp.int32, (1, outer), 1)
    low = lax.broadcasted_iota(jnp.int32, (1, inner), 1)
    high_angle = step * ((inner * high * channel) % frame_len).astype(jnp.float32)
    low_angle = step * ((low * channel) % frame_len).astype(jnp.float32)
    cos_high = jnp.cos(high_angle)
    sin_high = jnp.sin(high_angle)
    first = jnp.where(part == 0, cos_high, -sin_high)
    second = jnp.where(part == 0, sin_high, cos_high)
    cos_low = jnp.cos(low_angle)
    sin_low = jnp.sin(low_angle)
    norming = 1.0 / math.sqrt(frame_len)
    table = (
        first[:, :, None] * cos_low[:, None, :] - second[:, :, None] * sin_low[:, None, :]
    ) * norming
    return table.reshape(cols, frame_len).astype(jnp.bfloat16)


def polyphase(extended, coefficients, frames):
    tap_count = coefficients.shape[0]
    running = jnp.zeros((extended.shape[0], frames, extended.shape[2]), jnp.float32)
    for tap_index in range(tap_count):
        running = running + coefficients[tap_index][None, None, :] * extended[
            :, tap_index : tap_index + frames, :
        ].astype(jnp.float32)
    return running.astype(jnp.bfloat16)


def exchange(blocks, axis, flip):
    count = lax.axis_size(axis)
    bit = lax.axis_index(axis) // flip % 2
    from_low = [(i, i ^ flip) for i in range(count) if i // flip % 2 == 0]
    from_high = [(i, i ^ flip) for i in range(count) if i // flip % 2 == 1]
    to_high = lax.ppermute(blocks[1], axis, from_low)
    to_low = lax.ppermute(blocks[0], axis, from_high)
    return jnp.where(bit == 0, blocks[0], blocks[1]) + to_high + to_low


def local(voltages, coefficients, beam_weights):
    n_tm = lax.axis_size("tm")
    n_feed = lax.axis_size("feed")
    feeds_here, samples = voltages.shape
    tap_count, frame_len = coefficients.shape
    frames_here = samples // frame_len
    total_frames = n_tm * frames_here
    per_dev = feeds_here // n_tm

    blocks = voltages.reshape(n_tm, per_dev, samples)
    blocks = lax.all_to_all(blocks, "tm", 0, 0, tiled=True)
    frames = blocks.reshape(n_tm, per_dev, frames_here, frame_len)
    frames = jnp.transpose(frames, (1, 0, 2, 3)).reshape(per_dev, total_frames, frame_len)
    padding = jnp.zeros((per_dev, tap_count - 1, frame_len), frames.dtype)
    extended = jnp.concatenate([frames, padding], axis=1)
    filtered = polyphase(extended, coefficients, total_frames)

    table = dft_rows(frame_len, n_tm)
    spectra = jnp.einsum(
        "jk,mk->jm",
        table,
        filtered.reshape(per_dev * total_frames, frame_len),
        preferred_element_type=jnp.float32,
    ).astype(jnp.bfloat16)
    cols = table.shape[0]
    group_cols = cols // n_tm
    per_group = group_cols // 2
    spectra = spectra.reshape(n_tm, group_cols, per_dev * total_frames)
    turned = lax.all_to_all(spectra, "tm", 0, 0, tiled=True)
    turned = turned.reshape(n_tm, per_group, 2, per_dev, total_frames)
    turned = jnp.transpose(turned, (1, 0, 3, 2, 4)).reshape(per_group, feeds_here, 2, total_frames)
    real_part = turned[:, :, 0]
    imag_part = turned[:, :, 1]
    for_real = jnp.stack([real_part, -imag_part], axis=2)
    for_imag = jnp.stack([imag_part, real_part], axis=2)
    paired = jnp.concatenate([for_real, for_imag], axis=3).reshape(
        per_group, feeds_here * 2, 2 * total_frames
    )
    per_out = beam_weights.shape[3] // n_feed
    weights = beam_weights.reshape(per_group, feeds_here * 2, n_feed, per_out)
    beams = jnp.einsum("ckjb,ckn->jcbn", weights, paired, preferred_element_type=jnp.float32)
    flip = 1
    while flip < n_feed:
        split = beams.reshape(-1, 2, *beams.shape[1:])
        beams = exchange((split[:, 0], split[:, 1]), "feed", flip)
        flip *= 2
    beams = beams.reshape(per_group, per_out, 2, total_frames)
    energy = jnp.sum(beams * beams, axis=2)
    binned = jnp.mean(
        energy.reshape(per_group, per_out, total_frames // INTEG, INTEG), axis=3
    )
    return jnp.transpose(binned, (2, 0, 1))


def solution(mesh):
    placed = (P("feed", "tm"), P(), P("tm", "feed", None, None))
    return jax.shard_map(
        local, mesh=mesh, in_specs=placed, out_specs=P(None, "tm", "feed"), check_vma=False
    )
```

```python
import math

import jax
import jax.numpy as jnp
from jax import lax
from jax.sharding import PartitionSpec as P

INTEG = 8


def dft_rows(frame_len, n_groups):
    channels = frame_len // 2
    inner = 64
    outer = frame_len // inner
    cols = 2 * channels
    col = lax.broadcasted_iota(jnp.int32, (cols, 1), 0)
    per_group = channels // n_groups
    group = col // (2 * per_group)
    channel = group * per_group + (col % (2 * per_group)) // 2
    part = col % 2
    step = 2.0 * math.pi / frame_len
    high = lax.broadcasted_iota(jnp.int32, (1, outer), 1)
    low = lax.broadcasted_iota(jnp.int32, (1, inner), 1)
    high_angle = step * ((inner * high * channel) % frame_len).astype(jnp.float32)
    low_angle = step * ((low * channel) % frame_len).astype(jnp.float32)
    cos_high = jnp.cos(high_angle)
    sin_high = jnp.sin(high_angle)
    first = jnp.where(part == 0, cos_high, -sin_high)
    second = jnp.where(part == 0, sin_high, cos_high)
    cos_low = jnp.cos(low_angle)
    sin_low = jnp.sin(low_angle)
    norming = 1.0 / math.sqrt(frame_len)
    table = (
        first[:, :, None] * cos_low[:, None, :] - second[:, :, None] * sin_low[:, None, :]
    ) * norming
    return table.reshape(cols, frame_len).astype(jnp.bfloat16)


def polyphase(extended, coefficients, frames):
    tap_count = coefficients.shape[0]
    running = jnp.zeros((extended.shape[0], frames, extended.shape[2]), jnp.float32)
    for tap_index in range(tap_count):
        running = running + coefficients[tap_index][None, None, :] * extended[
            :, tap_index : tap_index + frames, :
        ].astype(jnp.float32)
    return running.astype(jnp.bfloat16)


def exchange(blocks, axis, flip):
    count = lax.axis_size(axis)
    low = lax.axis_index(axis) // flip % 2 == 0
    pairs = [(i, i ^ flip) for i in range(count)]
    received = lax.ppermute(jnp.where(low, blocks[1], blocks[0]), axis, pairs)
    return jnp.where(low, blocks[0], blocks[1]) + received


def local(voltages, coefficients, beam_weights):
    n_tm = lax.axis_size("tm")
    n_feed = lax.axis_size("feed")
    feeds_here, samples = voltages.shape
    tap_count, frame_len = coefficients.shape
    frames_here = samples // frame_len
    total_frames = n_tm * frames_here
    per_dev = feeds_here // n_tm

    blocks = voltages.reshape(n_tm, per_dev, samples)
    blocks = lax.all_to_all(blocks, "tm", 0, 0, tiled=True)
    frames = blocks.reshape(n_tm, per_dev, frames_here, frame_len)
    frames = jnp.transpose(frames, (1, 0, 2, 3)).reshape(per_dev, total_frames, frame_len)
    padding = jnp.zeros((per_dev, tap_count - 1, frame_len), frames.dtype)
    extended = jnp.concatenate([frames, padding], axis=1)
    filtered = polyphase(extended, coefficients, total_frames)

    table = dft_rows(frame_len, n_tm)
    spectra = jnp.einsum(
        "jk,mk->jm",
        table,
        filtered.reshape(per_dev * total_frames, frame_len),
        preferred_element_type=jnp.float32,
    ).astype(jnp.bfloat16)
    cols = table.shape[0]
    group_cols = cols // n_tm
    per_group = group_cols // 2
    spectra = spectra.reshape(n_tm, group_cols, per_dev * total_frames)
    turned = lax.all_to_all(spectra, "tm", 0, 0, tiled=True)
    turned = turned.reshape(n_tm, per_group, 2, per_dev, total_frames)
    turned = jnp.transpose(turned, (1, 0, 3, 2, 4)).reshape(per_group, feeds_here, 2, total_frames)
    real_part = turned[:, :, 0]
    imag_part = turned[:, :, 1]
    for_real = jnp.stack([real_part, -imag_part], axis=2)
    for_imag = jnp.stack([imag_part, real_part], axis=2)
    paired = jnp.concatenate([for_real, for_imag], axis=3).reshape(
        per_group, feeds_here * 2, 2 * total_frames
    )
    per_out = beam_weights.shape[3] // n_feed
    weights = beam_weights.reshape(per_group, feeds_here * 2, n_feed, per_out)
    beams = jnp.einsum("ckjb,ckn->jcbn", weights, paired, preferred_element_type=jnp.float32)
    flip = 1
    while flip < n_feed:
        split = beams.reshape(-1, 2, *beams.shape[1:])
        beams = exchange((split[:, 0], split[:, 1]), "feed", flip)
        flip *= 2
    beams = beams.reshape(per_group, per_out, 2, total_frames)
    energy = jnp.sum(beams * beams, axis=2)
    binned = jnp.mean(
        energy.reshape(per_group, per_out, total_frames // INTEG, INTEG), axis=3
    )
    return jnp.transpose(binned, (2, 0, 1))


def solution(mesh):
    placed = (P("feed", "tm"), P(), P("tm", "feed", None, None))
    return jax.shard_map(
        local, mesh=mesh, in_specs=placed, out_specs=P(None, "tm", "feed"), check_vma=False
    )
```

```python
import math

import jax
import jax.numpy as jnp
from jax import lax
from jax.sharding import PartitionSpec as P

INTEG = 8


def dft_rows(frame_len, n_groups):
    channels = frame_len // 2
    inner = 64
    outer = frame_len // inner
    cols = 2 * channels
    col = lax.broadcasted_iota(jnp.int32, (cols, 1), 0)
    per_group = channels // n_groups
    group = col // (2 * per_group)
    channel = group * per_group + (col % (2 * per_group)) // 2
    part = col % 2
    step = 2.0 * math.pi / frame_len
    high = lax.broadcasted_iota(jnp.int32, (1, outer), 1)
    low = lax.broadcasted_iota(jnp.int32, (1, inner), 1)
    high_angle = step * ((inner * high * channel) % frame_len).astype(jnp.float32)
    low_angle = step * ((low * channel) % frame_len).astype(jnp.float32)
    cos_high = jnp.cos(high_angle)
    sin_high = jnp.sin(high_angle)
    first = jnp.where(part == 0, cos_high, -sin_high)
    second = jnp.where(part == 0, sin_high, cos_high)
    cos_low = jnp.cos(low_angle)
    sin_low = jnp.sin(low_angle)
    norming = 1.0 / math.sqrt(frame_len)
    table = (
        first[:, :, None] * cos_low[:, None, :] - second[:, :, None] * sin_low[:, None, :]
    ) * norming
    return table.reshape(cols, frame_len).astype(jnp.bfloat16)


def polyphase(extended, coefficients, frames):
    tap_count = coefficients.shape[0]
    running = jnp.zeros((extended.shape[0], frames, extended.shape[2]), jnp.float32)
    for tap_index in range(tap_count):
        running = running + coefficients[tap_index][None, None, :] * extended[
            :, tap_index : tap_index + frames, :
        ].astype(jnp.float32)
    return running.astype(jnp.bfloat16)


def exchange(blocks, axis, flip):
    count = lax.axis_size(axis)
    low = lax.axis_index(axis) // flip % 2 == 0
    pairs = [(i, i ^ flip) for i in range(count)]
    received = lax.ppermute(jnp.where(low, blocks[1], blocks[0]), axis, pairs)
    return jnp.where(low, blocks[0], blocks[1]) + received


def local(voltages, coefficients, beam_weights):
    n_tm = lax.axis_size("tm")
    n_feed = lax.axis_size("feed")
    feeds_here, samples = voltages.shape
    tap_count, frame_len = coefficients.shape
    frames_here = samples // frame_len
    total_frames = n_tm * frames_here
    per_dev = feeds_here // n_tm

    blocks = voltages.reshape(n_tm, per_dev, samples)
    blocks = lax.all_to_all(blocks, "tm", 0, 0, tiled=True)
    frames = blocks.reshape(n_tm, per_dev, frames_here, frame_len)
    frames = jnp.transpose(frames, (1, 0, 2, 3)).reshape(per_dev, total_frames, frame_len)
    padding = jnp.zeros((per_dev, tap_count - 1, frame_len), frames.dtype)
    extended = jnp.concatenate([frames, padding], axis=1)
    filtered = polyphase(extended, coefficients, total_frames)

    table = dft_rows(frame_len, n_tm)
    spectra = jnp.einsum(
        "jk,mk->jm",
        table,
        filtered.reshape(per_dev * total_frames, frame_len),
        preferred_element_type=jnp.float32,
    ).astype(jnp.bfloat16)
    cols = table.shape[0]
    group_cols = cols // n_tm
    per_group = group_cols // 2
    spectra = spectra.reshape(n_tm, group_cols, per_dev * total_frames)
    turned = lax.all_to_all(spectra, "tm", 0, 0, tiled=True)
    turned = turned.reshape(n_tm, per_group, 2, per_dev, total_frames)
    turned = jnp.transpose(turned, (1, 0, 3, 2, 4)).reshape(per_group, feeds_here, 2, total_frames)
    real_part = turned[:, :, 0]
    imag_part = turned[:, :, 1]
    for_real = jnp.stack([real_part, -imag_part], axis=2)
    for_imag = jnp.stack([imag_part, real_part], axis=2)
    paired = jnp.concatenate([for_real, for_imag], axis=3).reshape(
        per_group, feeds_here * 2, 2 * total_frames
    )
    per_out = beam_weights.shape[3] // n_feed
    weights = beam_weights.reshape(per_group, feeds_here * 2, n_feed, per_out)
    n_parts = 2
    per_part = per_group // n_parts
    binned_parts = []
    for part in range(n_parts):
        chosen = slice(part * per_part, (part + 1) * per_part)
        beams = jnp.einsum(
            "ckjb,ckn->jcbn", weights[chosen], paired[chosen], preferred_element_type=jnp.float32
        )
        flip = 1
        while flip < n_feed:
            split = beams.reshape(-1, 2, *beams.shape[1:])
            beams = exchange((split[:, 0], split[:, 1]), "feed", flip)
            flip *= 2
        beams = beams.reshape(per_part, per_out, 2, total_frames)
        energy = jnp.sum(beams * beams, axis=2)
        binned_parts.append(
            jnp.mean(energy.reshape(per_part, per_out, total_frames // INTEG, INTEG), axis=3)
        )
    binned = jnp.concatenate(binned_parts, axis=0)
    return jnp.transpose(binned, (2, 0, 1))


def solution(mesh):
    placed = (P("feed", "tm"), P(), P("tm", "feed", None, None))
    return jax.shard_map(
        local, mesh=mesh, in_specs=placed, out_specs=P(None, "tm", "feed"), check_vma=False
    )
```

```python
import math

import jax
import jax.numpy as jnp
from jax import lax
from jax.sharding import PartitionSpec as P

INTEG = 8


def dft_rows(frame_len, n_groups):
    channels = frame_len // 2
    inner = 64
    outer = frame_len // inner
    cols = 2 * channels
    col = lax.broadcasted_iota(jnp.int32, (cols, 1), 0)
    per_group = channels // n_groups
    group = col // (2 * per_group)
    channel = group * per_group + (col % (2 * per_group)) // 2
    part = col % 2
    step = 2.0 * math.pi / frame_len
    high = lax.broadcasted_iota(jnp.int32, (1, outer), 1)
    low = lax.broadcasted_iota(jnp.int32, (1, inner), 1)
    high_angle = step * ((inner * high * channel) % frame_len).astype(jnp.float32)
    low_angle = step * ((low * channel) % frame_len).astype(jnp.float32)
    cos_high = jnp.cos(high_angle)
    sin_high = jnp.sin(high_angle)
    first = jnp.where(part == 0, cos_high, -sin_high)
    second = jnp.where(part == 0, sin_high, cos_high)
    cos_low = jnp.cos(low_angle)
    sin_low = jnp.sin(low_angle)
    norming = 1.0 / math.sqrt(frame_len)
    table = (
        first[:, :, None] * cos_low[:, None, :] - second[:, :, None] * sin_low[:, None, :]
    ) * norming
    return table.reshape(cols, frame_len).astype(jnp.bfloat16)


def polyphase(extended, coefficients, frames):
    tap_count = coefficients.shape[0]
    running = jnp.zeros((frames,) + extended.shape[1:], jnp.float32)
    for tap_index in range(tap_count):
        running = running + coefficients[tap_index][None, None, :] * extended[
            tap_index : tap_index + frames
        ].astype(jnp.float32)
    return running.astype(jnp.bfloat16)


def exchange(blocks, axis, flip):
    count = lax.axis_size(axis)
    low = lax.axis_index(axis) // flip % 2 == 0
    pairs = [(i, i ^ flip) for i in range(count)]
    received = lax.ppermute(jnp.where(low, blocks[1], blocks[0]), axis, pairs)
    return jnp.where(low, blocks[0], blocks[1]) + received


def local(voltages, coefficients, beam_weights):
    n_tm = lax.axis_size("tm")
    n_feed = lax.axis_size("feed")
    feeds_here, samples = voltages.shape
    tap_count, frame_len = coefficients.shape
    frames_here = samples // frame_len
    total_frames = n_tm * frames_here
    per_dev = feeds_here // n_tm

    blocks = voltages.reshape(n_tm, per_dev, samples)
    blocks = lax.all_to_all(blocks, "tm", 0, 0, tiled=True)
    frames = jnp.transpose(
        blocks.reshape(n_tm, per_dev, frames_here, frame_len), (0, 2, 1, 3)
    ).reshape(total_frames, per_dev, frame_len)
    padding = jnp.zeros((tap_count - 1, per_dev, frame_len), frames.dtype)
    extended = jnp.concatenate([frames, padding], axis=0)
    filtered = polyphase(extended, coefficients, total_frames)
    filtered = jnp.transpose(filtered, (1, 0, 2))

    table = dft_rows(frame_len, n_tm)
    spectra = jnp.einsum(
        "jk,mk->jm",
        table,
        filtered.reshape(per_dev * total_frames, frame_len),
        preferred_element_type=jnp.float32,
    ).astype(jnp.bfloat16)
    cols = table.shape[0]
    group_cols = cols // n_tm
    per_group = group_cols // 2
    spectra = spectra.reshape(n_tm, group_cols, per_dev * total_frames)
    turned = lax.all_to_all(spectra, "tm", 0, 0, tiled=True)
    turned = turned.reshape(n_tm, per_group, 2, per_dev, total_frames)
    turned = jnp.transpose(turned, (1, 0, 3, 2, 4)).reshape(per_group, feeds_here, 2, total_frames)
    real_part = turned[:, :, 0]
    imag_part = turned[:, :, 1]
    for_real = jnp.stack([real_part, -imag_part], axis=2)
    for_imag = jnp.stack([imag_part, real_part], axis=2)
    paired = jnp.concatenate([for_real, for_imag], axis=3).reshape(
        per_group, feeds_here * 2, 2 * total_frames
    )
    per_out = beam_weights.shape[3] // n_feed
    weights = beam_weights.reshape(per_group, feeds_here * 2, n_feed, per_out)
    n_parts = 2
    per_part = per_group // n_parts
    binned_parts = []
    for part in range(n_parts):
        chosen = slice(part * per_part, (part + 1) * per_part)
        beams = jnp.einsum(
            "ckjb,ckn->jcbn", weights[chosen], paired[chosen], preferred_element_type=jnp.float32
        )
        flip = 1
        while flip < n_feed:
            split = beams.reshape(-1, 2, *beams.shape[1:])
            beams = exchange((split[:, 0], split[:, 1]), "feed", flip)
            flip *= 2
        beams = beams.reshape(per_part, per_out, 2, total_frames)
        energy = jnp.sum(beams * beams, axis=2)
        binned_parts.append(
            jnp.mean(energy.reshape(per_part, per_out, total_frames // INTEG, INTEG), axis=3)
        )
    binned = jnp.concatenate(binned_parts, axis=0)
    return jnp.transpose(binned, (2, 0, 1))


def solution(mesh):
    placed = (P("feed", "tm"), P(), P("tm", "feed", None, None))
    return jax.shard_map(
        local, mesh=mesh, in_specs=placed, out_specs=P(None, "tm", "feed"), check_vma=False
    )
```

```python
import math

import jax
import jax.numpy as jnp
from jax import lax
from jax.sharding import PartitionSpec as P

INTEG = 8


def dft_rows(frame_len, n_groups):
    channels = frame_len // 2
    inner = 64
    outer = frame_len // inner
    cols = 2 * channels
    col = lax.broadcasted_iota(jnp.int32, (cols, 1), 0)
    per_group = channels // n_groups
    group = col // (2 * per_group)
    channel = group * per_group + (col % (2 * per_group)) // 2
    part = col % 2
    step = 2.0 * math.pi / frame_len
    high = lax.broadcasted_iota(jnp.int32, (1, outer), 1)
    low = lax.broadcasted_iota(jnp.int32, (1, inner), 1)
    high_angle = step * ((inner * high * channel) % frame_len).astype(jnp.float32)
    low_angle = step * ((low * channel) % frame_len).astype(jnp.float32)
    cos_high = jnp.cos(high_angle)
    sin_high = jnp.sin(high_angle)
    first = jnp.where(part == 0, cos_high, -sin_high)
    second = jnp.where(part == 0, sin_high, cos_high)
    cos_low = jnp.cos(low_angle)
    sin_low = jnp.sin(low_angle)
    norming = 1.0 / math.sqrt(frame_len)
    table = (
        first[:, :, None] * cos_low[:, None, :] - second[:, :, None] * sin_low[:, None, :]
    ) * norming
    return table.reshape(cols, frame_len).astype(jnp.bfloat16)


def polyphase(extended, coefficients, frames):
    tap_count = coefficients.shape[0]
    running = jnp.zeros((frames,) + extended.shape[1:], jnp.float32)
    for tap_index in range(tap_count):
        running = running + coefficients[tap_index][None, None, :] * extended[
            tap_index : tap_index + frames
        ].astype(jnp.float32)
    return running.astype(jnp.bfloat16)


def exchange(blocks, axis, flip):
    count = lax.axis_size(axis)
    low = lax.axis_index(axis) // flip % 2 == 0
    pairs = [(i, i ^ flip) for i in range(count)]
    received = lax.ppermute(jnp.where(low, blocks[1], blocks[0]), axis, pairs)
    return jnp.where(low, blocks[0], blocks[1]) + received


def local(voltages, coefficients, beam_weights):
    n_tm = lax.axis_size("tm")
    n_feed = lax.axis_size("feed")
    feeds_here, samples = voltages.shape
    tap_count, frame_len = coefficients.shape
    frames_here = samples // frame_len
    total_frames = n_tm * frames_here
    per_dev = feeds_here // n_tm

    blocks = voltages.reshape(n_tm, per_dev, samples)
    blocks = lax.all_to_all(blocks, "tm", 0, 0, tiled=True)
    frames = jnp.transpose(
        blocks.reshape(n_tm, per_dev, frames_here, frame_len), (0, 2, 1, 3)
    ).reshape(total_frames, per_dev, frame_len)
    padding = jnp.zeros((tap_count - 1, per_dev, frame_len), frames.dtype)
    extended = jnp.concatenate([frames, padding], axis=0)
    filtered = polyphase(extended, coefficients, total_frames)
    filtered = jnp.transpose(filtered, (1, 0, 2))

    table = dft_rows(frame_len, n_tm)
    spectra = jnp.einsum(
        "jk,mk->jm",
        table,
        filtered.reshape(per_dev * total_frames, frame_len),
        preferred_element_type=jnp.float32,
    ).astype(jnp.bfloat16)
    cols = table.shape[0]
    group_cols = cols // n_tm
    per_group = group_cols // 2
    spectra = spectra.reshape(n_tm, group_cols, per_dev * total_frames)
    turned = lax.all_to_all(spectra, "tm", 0, 0, tiled=True)
    turned = turned.reshape(n_tm, per_group, 2, per_dev, total_frames)
    turned = jnp.transpose(turned, (1, 0, 3, 2, 4)).reshape(per_group, feeds_here, 2, total_frames)
    real_part = turned[:, :, 0]
    imag_part = turned[:, :, 1]
    for_real = jnp.stack([real_part, -imag_part], axis=2)
    for_imag = jnp.stack([imag_part, real_part], axis=2)
    paired = jnp.concatenate([for_real, for_imag], axis=3).reshape(
        per_group, feeds_here * 2, 2 * total_frames
    )
    per_out = beam_weights.shape[3] // n_feed
    weights = beam_weights.reshape(per_group, feeds_here * 2, n_feed, per_out)
    n_parts = 4
    per_part = per_group // n_parts
    binned_parts = []
    for part in range(n_parts):
        chosen = slice(part * per_part, (part + 1) * per_part)
        beams = jnp.einsum(
            "ckjb,ckn->jcbn", weights[chosen], paired[chosen], preferred_element_type=jnp.float32
        )
        flip = 1
        while flip < n_feed:
            split = beams.reshape(-1, 2, *beams.shape[1:])
            beams = exchange((split[:, 0], split[:, 1]), "feed", flip)
            flip *= 2
        beams = beams.reshape(per_part, per_out, 2, total_frames)
        energy = jnp.sum(beams * beams, axis=2)
        binned_parts.append(
            jnp.mean(energy.reshape(per_part, per_out, total_frames // INTEG, INTEG), axis=3)
        )
    binned = jnp.concatenate(binned_parts, axis=0)
    return jnp.transpose(binned, (2, 0, 1))


def solution(mesh):
    placed = (P("feed", "tm"), P(), P("tm", "feed", None, None))
    return jax.shard_map(
        local, mesh=mesh, in_specs=placed, out_specs=P(None, "tm", "feed"), check_vma=False
    )
```

```python
import math

import jax
import jax.numpy as jnp
from jax import lax
from jax.sharding import PartitionSpec as P

INTEG = 8


def dft_rows(frame_len, n_groups):
    channels = frame_len // 2
    inner = 64
    outer = frame_len // inner
    cols = 2 * channels
    col = lax.broadcasted_iota(jnp.int32, (cols, 1), 0)
    per_group = channels // n_groups
    group = col // (2 * per_group)
    channel = group * per_group + (col % (2 * per_group)) // 2
    part = col % 2
    step = 2.0 * math.pi / frame_len
    high = lax.broadcasted_iota(jnp.int32, (1, outer), 1)
    low = lax.broadcasted_iota(jnp.int32, (1, inner), 1)
    high_angle = step * ((inner * high * channel) % frame_len).astype(jnp.float32)
    low_angle = step * ((low * channel) % frame_len).astype(jnp.float32)
    cos_high = jnp.cos(high_angle)
    sin_high = jnp.sin(high_angle)
    first = jnp.where(part == 0, cos_high, -sin_high)
    second = jnp.where(part == 0, sin_high, cos_high)
    cos_low = jnp.cos(low_angle)
    sin_low = jnp.sin(low_angle)
    norming = 1.0 / math.sqrt(frame_len)
    table = (
        first[:, :, None] * cos_low[:, None, :] - second[:, :, None] * sin_low[:, None, :]
    ) * norming
    return table.reshape(cols, frame_len).astype(jnp.bfloat16)


def polyphase(extended, coefficients, frames):
    tap_count = coefficients.shape[0]
    widened = extended.astype(jnp.float32)
    running = jnp.zeros((frames,) + extended.shape[1:], jnp.float32)
    for tap_index in range(tap_count):
        running = running + coefficients[tap_index][None, None, :] * widened[
            tap_index : tap_index + frames
        ]
    return running.astype(jnp.bfloat16)


def exchange(blocks, axis, flip):
    count = lax.axis_size(axis)
    low = lax.axis_index(axis) // flip % 2 == 0
    pairs = [(i, i ^ flip) for i in range(count)]
    received = lax.ppermute(jnp.where(low, blocks[1], blocks[0]), axis, pairs)
    return jnp.where(low, blocks[0], blocks[1]) + received


def local(voltages, coefficients, beam_weights):
    n_tm = lax.axis_size("tm")
    n_feed = lax.axis_size("feed")
    feeds_here, samples = voltages.shape
    tap_count, frame_len = coefficients.shape
    frames_here = samples // frame_len
    total_frames = n_tm * frames_here
    per_dev = feeds_here // n_tm

    blocks = voltages.reshape(n_tm, per_dev, samples)
    blocks = lax.all_to_all(blocks, "tm", 0, 0, tiled=True)
    frames = jnp.transpose(
        blocks.reshape(n_tm, per_dev, frames_here, frame_len), (0, 2, 1, 3)
    ).reshape(total_frames, per_dev, frame_len)
    padding = jnp.zeros((tap_count - 1, per_dev, frame_len), frames.dtype)
    extended = jnp.concatenate([frames, padding], axis=0)
    filtered = polyphase(extended, coefficients, total_frames)
    filtered = jnp.transpose(filtered, (1, 0, 2))

    table = dft_rows(frame_len, n_tm)
    spectra = jnp.einsum(
        "jk,mk->jm",
        table,
        filtered.reshape(per_dev * total_frames, frame_len),
        preferred_element_type=jnp.float32,
    ).astype(jnp.bfloat16)
    cols = table.shape[0]
    group_cols = cols // n_tm
    per_group = group_cols // 2
    spectra = spectra.reshape(n_tm, group_cols, per_dev * total_frames)
    turned = lax.all_to_all(spectra, "tm", 0, 0, tiled=True)
    turned = turned.reshape(n_tm, per_group, 2, per_dev, total_frames)
    turned = jnp.transpose(turned, (1, 0, 3, 2, 4)).reshape(per_group, feeds_here, 2, total_frames)
    real_part = turned[:, :, 0]
    imag_part = turned[:, :, 1]
    for_real = jnp.stack([real_part, -imag_part], axis=2)
    for_imag = jnp.stack([imag_part, real_part], axis=2)
    paired = jnp.concatenate([for_real, for_imag], axis=3).reshape(
        per_group, feeds_here * 2, 2 * total_frames
    )
    per_out = beam_weights.shape[3] // n_feed
    weights = beam_weights.reshape(per_group, feeds_here * 2, n_feed, per_out)
    n_parts = 2
    per_part = per_group // n_parts
    binned_parts = []
    for part in range(n_parts):
        chosen = slice(part * per_part, (part + 1) * per_part)
        beams = jnp.einsum(
            "ckjb,ckn->jcbn", weights[chosen], paired[chosen], preferred_element_type=jnp.float32
        )
        flip = 1
        while flip < n_feed:
            split = beams.reshape(-1, 2, *beams.shape[1:])
            beams = exchange((split[:, 0], split[:, 1]), "feed", flip)
            flip *= 2
        beams = beams.reshape(per_part, per_out, 2, total_frames)
        energy = jnp.sum(beams * beams, axis=2)
        binned_parts.append(
            jnp.mean(energy.reshape(per_part, per_out, total_frames // INTEG, INTEG), axis=3)
        )
    binned = jnp.concatenate(binned_parts, axis=0)
    return jnp.transpose(binned, (2, 0, 1))


def solution(mesh):
    placed = (P("feed", "tm"), P(), P("tm", "feed", None, None))
    return jax.shard_map(
        local, mesh=mesh, in_specs=placed, out_specs=P(None, "tm", "feed"), check_vma=False
    )
```

```python
import math

import jax
import jax.numpy as jnp
from jax import lax
from jax.sharding import PartitionSpec as P

INTEG = 8


def dft_rows(frame_len, n_groups):
    channels = frame_len // 2
    inner = 64
    outer = frame_len // inner
    cols = 2 * channels
    col = lax.broadcasted_iota(jnp.int32, (cols, 1), 0)
    per_group = channels // n_groups
    group = col // (2 * per_group)
    channel = group * per_group + (col % (2 * per_group)) // 2
    part = col % 2
    step = 2.0 * math.pi / frame_len
    high = lax.broadcasted_iota(jnp.int32, (1, outer), 1)
    low = lax.broadcasted_iota(jnp.int32, (1, inner), 1)
    high_angle = step * ((inner * high * channel) % frame_len).astype(jnp.float32)
    low_angle = step * ((low * channel) % frame_len).astype(jnp.float32)
    cos_high = jnp.cos(high_angle)
    sin_high = jnp.sin(high_angle)
    first = jnp.where(part == 0, cos_high, -sin_high)
    second = jnp.where(part == 0, sin_high, cos_high)
    cos_low = jnp.cos(low_angle)
    sin_low = jnp.sin(low_angle)
    norming = 1.0 / math.sqrt(frame_len)
    table = (
        first[:, :, None] * cos_low[:, None, :] - second[:, :, None] * sin_low[:, None, :]
    ) * norming
    return table.reshape(cols, frame_len).astype(jnp.bfloat16)


def polyphase(extended, coefficients, frames):
    tap_count = coefficients.shape[0]
    widened = extended.astype(jnp.float32)
    running = jnp.zeros((frames,) + extended.shape[1:], jnp.float32)
    for tap_index in range(tap_count):
        running = running + coefficients[tap_index][None, None, :] * widened[
            tap_index : tap_index + frames
        ]
    return running.astype(jnp.bfloat16)


def exchange(blocks, axis, flip):
    count = lax.axis_size(axis)
    low = lax.axis_index(axis) // flip % 2 == 0
    pairs = [(i, i ^ flip) for i in range(count)]
    received = lax.ppermute(jnp.where(low, blocks[1], blocks[0]), axis, pairs)
    return jnp.where(low, blocks[0], blocks[1]) + received


def local(voltages, coefficients, beam_weights):
    n_tm = lax.axis_size("tm")
    n_feed = lax.axis_size("feed")
    feeds_here, samples = voltages.shape
    tap_count, frame_len = coefficients.shape
    frames_here = samples // frame_len
    total_frames = n_tm * frames_here
    per_dev = feeds_here // n_tm

    blocks = voltages.reshape(n_tm, per_dev, samples)
    blocks = lax.all_to_all(blocks, "tm", 0, 0, tiled=True)
    frames = jnp.transpose(
        blocks.reshape(n_tm, per_dev, frames_here, frame_len), (0, 2, 1, 3)
    ).reshape(total_frames, per_dev, frame_len)
    padding = jnp.zeros((tap_count - 1, per_dev, frame_len), frames.dtype)
    extended = jnp.concatenate([frames, padding], axis=0)
    filtered = polyphase(extended, coefficients, total_frames)
    filtered = jnp.transpose(filtered, (1, 0, 2))

    table = dft_rows(frame_len, n_tm)
    spectra = jnp.einsum(
        "jk,mk->jm",
        table,
        filtered.reshape(per_dev * total_frames, frame_len),
        preferred_element_type=jnp.float32,
    ).astype(jnp.bfloat16)
    cols = table.shape[0]
    group_cols = cols // n_tm
    per_group = group_cols // 2
    spectra = spectra.reshape(n_tm, group_cols, per_dev * total_frames)
    turned = lax.all_to_all(spectra, "tm", 0, 0, tiled=True)
    turned = turned.reshape(n_tm, per_group, 2, per_dev, total_frames)
    turned = jnp.transpose(turned, (1, 0, 3, 2, 4)).reshape(per_group, feeds_here, 2, total_frames)
    real_part = turned[:, :, 0]
    imag_part = turned[:, :, 1]
    for_real = jnp.stack([real_part, -imag_part], axis=2)
    for_imag = jnp.stack([imag_part, real_part], axis=2)
    paired = jnp.concatenate([for_real, for_imag], axis=3).reshape(
        per_group, feeds_here * 2, 2 * total_frames
    )
    per_out = beam_weights.shape[3] // n_feed
    weights = beam_weights.reshape(per_group, feeds_here * 2, n_feed, per_out)
    beams_all = jnp.einsum("ckjb,ckn->jcbn", weights, paired, preferred_element_type=jnp.float32)
    n_parts = 2
    per_part = per_group // n_parts
    binned_parts = []
    for part in range(n_parts):
        beams = beams_all[:, part * per_part : (part + 1) * per_part]
        flip = 1
        while flip < n_feed:
            split = beams.reshape(-1, 2, *beams.shape[1:])
            beams = exchange((split[:, 0], split[:, 1]), "feed", flip)
            flip *= 2
        beams = beams.reshape(per_part, per_out, 2, total_frames)
        energy = jnp.sum(beams * beams, axis=2)
        binned_parts.append(
            jnp.mean(energy.reshape(per_part, per_out, total_frames // INTEG, INTEG), axis=3)
        )
    binned = jnp.concatenate(binned_parts, axis=0)
    return jnp.transpose(binned, (2, 0, 1))


def solution(mesh):
    placed = (P("feed", "tm"), P(), P("tm", "feed", None, None))
    return jax.shard_map(
        local, mesh=mesh, in_specs=placed, out_specs=P(None, "tm", "feed"), check_vma=False
    )
```

```python
import math

import jax
import jax.numpy as jnp
from jax import lax
from jax.sharding import PartitionSpec as P

INTEG = 8


def dft_rows(frame_len, n_groups):
    channels = frame_len // 2
    inner = 64
    outer = frame_len // inner
    cols = 2 * channels
    col = lax.broadcasted_iota(jnp.int32, (cols, 1), 0)
    per_group = channels // n_groups
    group = col // (2 * per_group)
    channel = group * per_group + (col % (2 * per_group)) // 2
    part = col % 2
    step = 2.0 * math.pi / frame_len
    high = lax.broadcasted_iota(jnp.int32, (1, outer), 1)
    low = lax.broadcasted_iota(jnp.int32, (1, inner), 1)
    high_angle = step * ((inner * high * channel) % frame_len).astype(jnp.float32)
    low_angle = step * ((low * channel) % frame_len).astype(jnp.float32)
    cos_high = jnp.cos(high_angle)
    sin_high = jnp.sin(high_angle)
    first = jnp.where(part == 0, cos_high, -sin_high)
    second = jnp.where(part == 0, sin_high, cos_high)
    cos_low = jnp.cos(low_angle)
    sin_low = jnp.sin(low_angle)
    norming = 1.0 / math.sqrt(frame_len)
    table = (
        first[:, :, None] * cos_low[:, None, :] - second[:, :, None] * sin_low[:, None, :]
    ) * norming
    return table.reshape(cols, frame_len).astype(jnp.bfloat16)


def polyphase(extended, coefficients, frames):
    tap_count = coefficients.shape[0]
    widened = extended.astype(jnp.float32)
    running = jnp.zeros((frames,) + extended.shape[1:], jnp.float32)
    for tap_index in range(tap_count):
        running = running + coefficients[tap_index][None, None, :] * widened[
            tap_index : tap_index + frames
        ]
    return running.astype(jnp.bfloat16)


def exchange(blocks, axis, flip):
    count = lax.axis_size(axis)
    low = lax.axis_index(axis) // flip % 2 == 0
    pairs = [(i, i ^ flip) for i in range(count)]
    received = lax.ppermute(jnp.where(low, blocks[1], blocks[0]), axis, pairs)
    return jnp.where(low, blocks[0], blocks[1]) + received


def local(voltages, coefficients, beam_weights):
    n_tm = lax.axis_size("tm")
    n_feed = lax.axis_size("feed")
    feeds_here, samples = voltages.shape
    tap_count, frame_len = coefficients.shape
    frames_here = samples // frame_len
    total_frames = n_tm * frames_here
    per_dev = feeds_here // n_tm

    blocks = voltages.reshape(n_tm, per_dev, samples)
    blocks = lax.all_to_all(blocks, "tm", 0, 0, tiled=True)
    per_out = beam_weights.shape[3] // n_feed
    weights = beam_weights.reshape(beam_weights.shape[0], feeds_here * 2, n_feed, per_out)
    blocks, weights = lax.optimization_barrier((blocks, weights))
    frames = jnp.transpose(
        blocks.reshape(n_tm, per_dev, frames_here, frame_len), (0, 2, 1, 3)
    ).reshape(total_frames, per_dev, frame_len)
    padding = jnp.zeros((tap_count - 1, per_dev, frame_len), frames.dtype)
    extended = jnp.concatenate([frames, padding], axis=0)
    filtered = polyphase(extended, coefficients, total_frames)
    filtered = jnp.transpose(filtered, (1, 0, 2))

    table = dft_rows(frame_len, n_tm)
    spectra = jnp.einsum(
        "jk,mk->jm",
        table,
        filtered.reshape(per_dev * total_frames, frame_len),
        preferred_element_type=jnp.float32,
    ).astype(jnp.bfloat16)
    cols = table.shape[0]
    group_cols = cols // n_tm
    per_group = group_cols // 2
    spectra = spectra.reshape(n_tm, group_cols, per_dev * total_frames)
    turned = lax.all_to_all(spectra, "tm", 0, 0, tiled=True)
    turned = turned.reshape(n_tm, per_group, 2, per_dev, total_frames)
    turned = jnp.transpose(turned, (1, 0, 3, 2, 4)).reshape(per_group, feeds_here, 2, total_frames)
    real_part = turned[:, :, 0]
    imag_part = turned[:, :, 1]
    for_real = jnp.stack([real_part, -imag_part], axis=2)
    for_imag = jnp.stack([imag_part, real_part], axis=2)
    paired = jnp.concatenate([for_real, for_imag], axis=3).reshape(
        per_group, feeds_here * 2, 2 * total_frames
    )
    beams_all = jnp.einsum("ckjb,ckn->jcbn", weights, paired, preferred_element_type=jnp.float32)
    n_parts = 2
    per_part = per_group // n_parts
    binned_parts = []
    for part in range(n_parts):
        beams = beams_all[:, part * per_part : (part + 1) * per_part]
        flip = 1
        while flip < n_feed:
            split = beams.reshape(-1, 2, *beams.shape[1:])
            beams = exchange((split[:, 0], split[:, 1]), "feed", flip)
            flip *= 2
        beams = beams.reshape(per_part, per_out, 2, total_frames)
        energy = jnp.sum(beams * beams, axis=2)
        binned_parts.append(
            jnp.mean(energy.reshape(per_part, per_out, total_frames // INTEG, INTEG), axis=3)
        )
    binned = jnp.concatenate(binned_parts, axis=0)
    return jnp.transpose(binned, (2, 0, 1))


def solution(mesh):
    placed = (P("feed", "tm"), P(), P("tm", "feed", None, None))
    return jax.shard_map(
        local, mesh=mesh, in_specs=placed, out_specs=P(None, "tm", "feed"), check_vma=False
    )
```

```python
import math

import jax
import jax.numpy as jnp
from jax import lax
from jax.sharding import PartitionSpec as P

INTEG = 8


def dft_rows(frame_len, n_groups):
    channels = frame_len // 2
    inner = 64
    outer = frame_len // inner
    cols = 2 * channels
    col = lax.broadcasted_iota(jnp.int32, (cols, 1), 0)
    per_group = channels // n_groups
    group = col // (2 * per_group)
    channel = group * per_group + (col % (2 * per_group)) // 2
    part = col % 2
    step = 2.0 * math.pi / frame_len
    high = lax.broadcasted_iota(jnp.int32, (1, outer), 1)
    low = lax.broadcasted_iota(jnp.int32, (1, inner), 1)
    high_angle = step * ((inner * high * channel) % frame_len).astype(jnp.float32)
    low_angle = step * ((low * channel) % frame_len).astype(jnp.float32)
    cos_high = jnp.cos(high_angle)
    sin_high = jnp.sin(high_angle)
    first = jnp.where(part == 0, cos_high, -sin_high)
    second = jnp.where(part == 0, sin_high, cos_high)
    cos_low = jnp.cos(low_angle)
    sin_low = jnp.sin(low_angle)
    norming = 1.0 / math.sqrt(frame_len)
    table = (
        first[:, :, None] * cos_low[:, None, :] - second[:, :, None] * sin_low[:, None, :]
    ) * norming
    return table.reshape(cols, frame_len).astype(jnp.bfloat16)


def polyphase(extended, coefficients, frames):
    tap_count = coefficients.shape[0]
    widened = extended.astype(jnp.float32)
    running = jnp.zeros((frames,) + extended.shape[1:], jnp.float32)
    for tap_index in range(tap_count):
        running = running + coefficients[tap_index][None, None, :] * widened[
            tap_index : tap_index + frames
        ]
    return running.astype(jnp.bfloat16)


def exchange(blocks, axis, flip):
    count = lax.axis_size(axis)
    low = lax.axis_index(axis) // flip % 2 == 0
    pairs = [(i, i ^ flip) for i in range(count)]
    received = lax.ppermute(jnp.where(low, blocks[1], blocks[0]), axis, pairs)
    return jnp.where(low, blocks[0], blocks[1]) + received


def local(voltages, coefficients, beam_weights):
    n_tm = lax.axis_size("tm")
    n_feed = lax.axis_size("feed")
    feeds_here, samples = voltages.shape
    tap_count, frame_len = coefficients.shape
    frames_here = samples // frame_len
    total_frames = n_tm * frames_here
    per_dev = feeds_here // n_tm

    blocks = voltages.reshape(n_tm, per_dev, samples)
    blocks = lax.all_to_all(blocks, "tm", 0, 0, tiled=True)
    frames = jnp.transpose(
        blocks.reshape(n_tm, per_dev, frames_here, frame_len), (0, 2, 1, 3)
    ).reshape(total_frames, per_dev, frame_len)
    padding = jnp.zeros((tap_count - 1, per_dev, frame_len), frames.dtype)
    extended = jnp.concatenate([frames, padding], axis=0)
    filtered = polyphase(extended, coefficients, total_frames)
    filtered = jnp.transpose(filtered, (1, 0, 2))

    table = dft_rows(frame_len, n_tm)
    spectra = jnp.einsum(
        "jk,mk->jm",
        table,
        filtered.reshape(per_dev * total_frames, frame_len),
        preferred_element_type=jnp.float32,
    ).astype(jnp.bfloat16)
    cols = table.shape[0]
    group_cols = cols // n_tm
    per_group = group_cols // 2
    spectra = spectra.reshape(n_tm, group_cols, per_dev * total_frames)
    turned = lax.all_to_all(spectra, "tm", 0, 0, tiled=True)
    turned = turned.reshape(n_tm, per_group, 2, per_dev, total_frames)
    turned = jnp.transpose(turned, (1, 0, 3, 2, 4)).reshape(per_group, feeds_here, 2, total_frames)
    real_part = turned[:, :, 0]
    imag_part = turned[:, :, 1]
    for_real = jnp.stack([real_part, -imag_part], axis=2)
    for_imag = jnp.stack([imag_part, real_part], axis=2)
    paired = jnp.concatenate([for_real, for_imag], axis=3).reshape(
        per_group, feeds_here * 2, 2 * total_frames
    )
    per_out = beam_weights.shape[3] // n_feed
    weights = beam_weights.reshape(per_group, feeds_here * 2, n_feed, per_out)
    beams_all = jnp.einsum("ckjb,ckn->jcbn", weights, paired, preferred_element_type=jnp.float32)
    n_parts = 4
    per_part = per_group // n_parts
    binned_parts = []
    for part in range(n_parts):
        beams = beams_all[:, part * per_part : (part + 1) * per_part]
        flip = 1
        while flip < n_feed:
            split = beams.reshape(-1, 2, *beams.shape[1:])
            beams = exchange((split[:, 0], split[:, 1]), "feed", flip)
            flip *= 2
        beams = beams.reshape(per_part, per_out, 2, total_frames)
        energy = jnp.sum(beams * beams, axis=2)
        binned_parts.append(
            jnp.mean(energy.reshape(per_part, per_out, total_frames // INTEG, INTEG), axis=3)
        )
    binned = jnp.concatenate(binned_parts, axis=0)
    return jnp.transpose(binned, (2, 0, 1))


def solution(mesh):
    placed = (P("feed", "tm"), P(), P("tm", "feed", None, None))
    return jax.shard_map(
        local, mesh=mesh, in_specs=placed, out_specs=P(None, "tm", "feed"), check_vma=False
    )
```

```python
import math

import jax
import jax.numpy as jnp
from jax import lax
from jax.sharding import PartitionSpec as P

INTEG = 8


def dft_rows(frame_len, n_groups):
    channels = frame_len // 2
    inner = 64
    outer = frame_len // inner
    cols = 2 * channels
    col = lax.broadcasted_iota(jnp.int32, (cols, 1), 0)
    per_group = channels // n_groups
    group = col // (2 * per_group)
    channel = group * per_group + (col % (2 * per_group)) // 2
    part = col % 2
    step = 2.0 * math.pi / frame_len
    high = lax.broadcasted_iota(jnp.int32, (1, outer), 1)
    low = lax.broadcasted_iota(jnp.int32, (1, inner), 1)
    high_angle = step * ((inner * high * channel) % frame_len).astype(jnp.float32)
    low_angle = step * ((low * channel) % frame_len).astype(jnp.float32)
    cos_high = jnp.cos(high_angle)
    sin_high = jnp.sin(high_angle)
    first = jnp.where(part == 0, cos_high, -sin_high)
    second = jnp.where(part == 0, sin_high, cos_high)
    cos_low = jnp.cos(low_angle)
    sin_low = jnp.sin(low_angle)
    norming = 1.0 / math.sqrt(frame_len)
    table = (
        first[:, :, None] * cos_low[:, None, :] - second[:, :, None] * sin_low[:, None, :]
    ) * norming
    return table.reshape(cols, frame_len).astype(jnp.bfloat16)


def polyphase(extended, coefficients, frames):
    tap_count = coefficients.shape[0]
    widened = extended.astype(jnp.float32)
    running = jnp.zeros((frames,) + extended.shape[1:], jnp.float32)
    for tap_index in range(tap_count):
        running = running + coefficients[tap_index][None, None, :] * widened[
            tap_index : tap_index + frames
        ]
    return running.astype(jnp.bfloat16)


def exchange(blocks, axis, flip):
    count = lax.axis_size(axis)
    low = lax.axis_index(axis) // flip % 2 == 0
    pairs = [(i, i ^ flip) for i in range(count)]
    received = lax.ppermute(jnp.where(low, blocks[1], blocks[0]), axis, pairs)
    return jnp.where(low, blocks[0], blocks[1]) + received


def local(voltages, coefficients, beam_weights):
    n_tm = lax.axis_size("tm")
    n_feed = lax.axis_size("feed")
    feeds_here, samples = voltages.shape
    tap_count, frame_len = coefficients.shape
    frames_here = samples // frame_len
    total_frames = n_tm * frames_here
    per_dev = feeds_here // n_tm

    blocks = voltages.reshape(n_tm, per_dev, samples)
    blocks = lax.all_to_all(blocks, "tm", 0, 0, tiled=True)
    frames = jnp.transpose(
        blocks.reshape(n_tm, per_dev, frames_here, frame_len), (0, 2, 1, 3)
    ).reshape(total_frames, per_dev, frame_len)
    padding = jnp.zeros((tap_count - 1, per_dev, frame_len), frames.dtype)
    extended = jnp.concatenate([frames, padding], axis=0)
    filtered = polyphase(extended, coefficients, total_frames)
    filtered = jnp.transpose(filtered, (1, 0, 2))

    table = dft_rows(frame_len, n_tm)
    spectra = jnp.einsum(
        "jk,mk->jm",
        table,
        filtered.reshape(per_dev * total_frames, frame_len),
        preferred_element_type=jnp.float32,
    ).astype(jnp.bfloat16)
    cols = table.shape[0]
    group_cols = cols // n_tm
    per_group = group_cols // 2
    spectra = spectra.reshape(n_tm, group_cols, per_dev * total_frames)
    turned = lax.all_to_all(spectra, "tm", 0, 0, tiled=True)
    turned = turned.reshape(n_tm, per_group, 2, per_dev, total_frames)
    turned = jnp.transpose(turned, (1, 0, 3, 2, 4)).reshape(per_group, feeds_here, 2, total_frames)
    real_part = turned[:, :, 0]
    imag_part = turned[:, :, 1]
    for_real = jnp.stack([real_part, -imag_part], axis=2)
    for_imag = jnp.stack([imag_part, real_part], axis=2)
    paired = jnp.concatenate([for_real, for_imag], axis=3).reshape(
        per_group, feeds_here * 2, 2 * total_frames
    )
    per_out = beam_weights.shape[3] // n_feed
    weights = beam_weights.reshape(per_group, feeds_here * 2, n_feed, per_out)
    beams_all = jnp.einsum("ckjb,ckn->jcbn", weights, paired, preferred_element_type=jnp.float32)
    n_parts = 8
    per_part = per_group // n_parts
    binned_parts = []
    for part in range(n_parts):
        beams = beams_all[:, part * per_part : (part + 1) * per_part]
        flip = 1
        while flip < n_feed:
            split = beams.reshape(-1, 2, *beams.shape[1:])
            beams = exchange((split[:, 0], split[:, 1]), "feed", flip)
            flip *= 2
        beams = beams.reshape(per_part, per_out, 2, total_frames)
        energy = jnp.sum(beams * beams, axis=2)
        binned_parts.append(
            jnp.mean(energy.reshape(per_part, per_out, total_frames // INTEG, INTEG), axis=3)
        )
    binned = jnp.concatenate(binned_parts, axis=0)
    return jnp.transpose(binned, (2, 0, 1))


def solution(mesh):
    placed = (P("feed", "tm"), P(), P("tm", "feed", None, None))
    return jax.shard_map(
        local, mesh=mesh, in_specs=placed, out_specs=P(None, "tm", "feed"), check_vma=False
    )
```

```python
import math

import jax
import jax.numpy as jnp
from jax import lax
from jax.sharding import PartitionSpec as P

INTEG = 8


def dft_rows(frame_len, n_groups):
    channels = frame_len // 2
    inner = 64
    outer = frame_len // inner
    cols = 2 * channels
    col = lax.broadcasted_iota(jnp.int32, (cols, 1), 0)
    per_group = channels // n_groups
    group = col // (2 * per_group)
    channel = group * per_group + (col % (2 * per_group)) // 2
    part = col % 2
    step = 2.0 * math.pi / frame_len
    high = lax.broadcasted_iota(jnp.int32, (1, outer), 1)
    low = lax.broadcasted_iota(jnp.int32, (1, inner), 1)
    high_angle = step * ((inner * high * channel) % frame_len).astype(jnp.float32)
    low_angle = step * ((low * channel) % frame_len).astype(jnp.float32)
    cos_high = jnp.cos(high_angle)
    sin_high = jnp.sin(high_angle)
    first = jnp.where(part == 0, cos_high, -sin_high)
    second = jnp.where(part == 0, sin_high, cos_high)
    cos_low = jnp.cos(low_angle)
    sin_low = jnp.sin(low_angle)
    norming = 1.0 / math.sqrt(frame_len)
    table = (
        first[:, :, None] * cos_low[:, None, :] - second[:, :, None] * sin_low[:, None, :]
    ) * norming
    return table.reshape(cols, frame_len).astype(jnp.bfloat16)


def polyphase(extended, coefficients, frames):
    tap_count = coefficients.shape[0]
    widened = extended.astype(jnp.float32)
    running = jnp.zeros((frames,) + extended.shape[1:], jnp.float32)
    for tap_index in range(tap_count):
        running = running + coefficients[tap_index][None, None, :] * widened[
            tap_index : tap_index + frames
        ]
    return running.astype(jnp.bfloat16)


def exchange(blocks, axis, flip):
    count = lax.axis_size(axis)
    low = lax.axis_index(axis) // flip % 2 == 0
    pairs = [(i, i ^ flip) for i in range(count)]
    received = lax.ppermute(jnp.where(low, blocks[1], blocks[0]), axis, pairs)
    return jnp.where(low, blocks[0], blocks[1]) + received


def local(voltages, coefficients, beam_weights):
    n_tm = lax.axis_size("tm")
    n_feed = lax.axis_size("feed")
    feeds_here, samples = voltages.shape
    tap_count, frame_len = coefficients.shape
    frames_here = samples // frame_len
    total_frames = n_tm * frames_here
    per_dev = feeds_here // n_tm

    blocks = voltages.reshape(n_tm, per_dev, samples)
    blocks = lax.all_to_all(blocks, "tm", 0, 0, tiled=True)
    frames = jnp.transpose(
        blocks.reshape(n_tm, per_dev, frames_here, frame_len), (0, 2, 1, 3)
    ).reshape(total_frames, per_dev, frame_len)
    padding = jnp.zeros((tap_count - 1, per_dev, frame_len), frames.dtype)
    extended = jnp.concatenate([frames, padding], axis=0)
    filtered = polyphase(extended, coefficients, total_frames)
    filtered = jnp.transpose(filtered, (1, 0, 2))

    table = dft_rows(frame_len, n_tm)
    spectra = jnp.einsum(
        "jk,mk->jm",
        table,
        filtered.reshape(per_dev * total_frames, frame_len),
        preferred_element_type=jnp.float32,
    ).astype(jnp.bfloat16)
    cols = table.shape[0]
    group_cols = cols // n_tm
    per_group = group_cols // 2
    spectra = spectra.reshape(n_tm, group_cols, per_dev * total_frames)
    turned = lax.all_to_all(spectra, "tm", 0, 0, tiled=True)
    turned = turned.reshape(n_tm, per_group, 2, per_dev, total_frames)
    turned = jnp.transpose(turned, (1, 0, 3, 2, 4)).reshape(per_group, feeds_here, 2, total_frames)
    real_part = turned[:, :, 0]
    imag_part = turned[:, :, 1]
    for_real = jnp.stack([real_part, -imag_part], axis=2)
    for_imag = jnp.stack([imag_part, real_part], axis=2)
    paired = jnp.concatenate([for_real, for_imag], axis=3).reshape(
        per_group, feeds_here * 2, 2 * total_frames
    )
    per_out = beam_weights.shape[3] // n_feed
    weights = beam_weights.reshape(per_group, feeds_here * 2, n_feed, per_out)
    beams_all = jnp.einsum("ckjb,ckn->jcbn", weights, paired, preferred_element_type=jnp.float32)
    bounds = [0, per_group // 8, per_group // 4, per_group // 2, per_group]
    binned_parts = []
    for start, stop in zip(bounds[:-1], bounds[1:]):
        per_part = stop - start
        beams = beams_all[:, start:stop]
        flip = 1
        while flip < n_feed:
            split = beams.reshape(-1, 2, *beams.shape[1:])
            beams = exchange((split[:, 0], split[:, 1]), "feed", flip)
            flip *= 2
        beams = beams.reshape(per_part, per_out, 2, total_frames)
        energy = jnp.sum(beams * beams, axis=2)
        binned_parts.append(
            jnp.mean(energy.reshape(per_part, per_out, total_frames // INTEG, INTEG), axis=3)
        )
    binned = jnp.concatenate(binned_parts, axis=0)
    return jnp.transpose(binned, (2, 0, 1))


def solution(mesh):
    placed = (P("feed", "tm"), P(), P("tm", "feed", None, None))
    return jax.shard_map(
        local, mesh=mesh, in_specs=placed, out_specs=P(None, "tm", "feed"), check_vma=False
    )
```
